128 devices in a mesh: img: 8 (over z_hi, y), cap: 16 (over x, z_lo, core).
Axes of the slice: x: 4, y: 4, z: 4 (z_hi: 2, z_lo: 2; z = z_hi * 2 + z_lo), core: 2. Of those that a mesh axis runs over, the one named last changes fastest.
Arguments:
- images: float32 [16384, 768], P('img'), may hold values from -100 to 100
- captions: float32 [16384, 768], P('cap', 'img'), may hold values from -8 to 8
- bank: float32 [16384, 768], P('img'), may hold values from -100 to 100
Outputs:
- expected: float32 [16384, 768], P('img')
The draws below stay inside these ranges and needn't reach their ends.
All inputs are finite; a program needn't handle non-finite values.
Results may differ from the reference program's by a relative error of at most 0.0003.
Values sent between devices are 32-bit elements; how exact they have to be, the bound alone decides.
No kernel may reach another device: no remote copies, remote signals or barrier semaphores. Data moves between devices by JAX's collectives and lax.ppermute only.
A program may use at most 448 MiB of HBM per device.

```python
import math
import jax
import jax.numpy as jnp
from jax import lax

D = 768
IMAGE_ROWS_LOCAL = 2048
BANK_DEV = 2048
NI = 16384
NC = 16384
NB = 16384
N_IMG = 8


def caption_table(key):
    first, second_input = jax.random.split(jax.random.fold_in(key, 11))
    raw = jnp.clip(jax.random.normal(first, (NC, D), jnp.float32), -4.0, 4.0)
    scale = jnp.exp(jax.random.uniform(second_input, (NC, 1), jnp.float32, math.log(0.5), math.log(2.0)))
    position = jnp.arange(NC, dtype=jnp.int32)[:, None]
    chosen = position % (NC // 8) < 4
    scale = jnp.where(chosen, jnp.float32(2.0), scale)
    return raw * scale


def embedding_rows(key, count, rising):
    first, second_input = jax.random.split(key)
    scale = jnp.exp(jax.random.uniform(second_input, (count, 1), jnp.float32, math.log(0.5), math.log(2.0)))
    if rising:
        scale = scale * jnp.exp(math.log(3.0) * jnp.arange(count, dtype=jnp.float32)[:, None] / count)
    raw = jnp.clip(jax.random.normal(first, (count, D), jnp.float32), -4.0, 4.0)
    return raw * scale


def plant(rows, key, offset):
    table = caption_table(key)
    for index in range(8):
        caption_vector = index * (NC // 8) + offset
        prior_power = 5.0 + index
        rows = rows.at[index].set(prior_power * 0.5 * (table[caption_vector] + table[caption_vector + 1]))
    return rows


def draw_captions(key, part):
    return caption_table(key)


def draw_images(key, part):
    rows = embedding_rows(jax.random.fold_in(key, 21), NI, False)
    return plant(rows, key, 0)


def draw_bank(key, part):
    rows = embedding_rows(jax.random.fold_in(key, 31), NB, True)
    return plant(rows, key, 2)


def setup_inputs(seed: int = 0) -> dict:
    key_of = jax.random.split(jax.random.key(seed), 4)
    images = draw_images(jax.random.fold_in(key_of[3], 71), 0)
    captions = draw_captions(jax.random.fold_in(key_of[3], 71), 0)
    bank = draw_bank(jax.random.fold_in(key_of[3], 71), 0)
    return dict(images=images, captions=captions, bank=bank)


exponent_divisor = 0.03


def similar(query_factor, target_factor):
    return exponent_divisor * lax.dot_general(query_factor, target_factor, (((1,), (1,)), ((), ())), precision=lax.Precision.HIGHEST, preferred_element_type=jnp.float32)


def reference(images, captions, bank):
    blocks = bank.reshape(N_IMG, BANK_DEV, D)

    def advance_caption_group(carry, block):
        peak, total = carry
        scores = similar(block, captions)
        newpeak = jnp.maximum(peak, jnp.max(scores, axis=0))
        total = total * jnp.exp(peak - newpeak) + jnp.sum(jnp.exp(scores - newpeak[None, :]), axis=0)
        return (newpeak, total), None

    start = (jnp.full((NC,), -1e30, jnp.float32), jnp.zeros((NC,), jnp.float32))
    (peak, total), ignored_argument = lax.scan(advance_caption_group, start, blocks)
    col_log = peak + jnp.log(total)

    def row_block(rows):
        logits = similar(rows, captions) - col_log[None, :]
        row_max = jnp.max(logits, axis=1, keepdims=True)
        weights = jnp.exp(logits - row_max)
        row_total = jnp.sum(weights, axis=1, keepdims=True)
        summed = jnp.dot(weights, captions, precision=lax.Precision.HIGHEST, preferred_element_type=jnp.float32)
        return summed / row_total

    result = lax.map(row_block, images.reshape(N_IMG, IMAGE_ROWS_LOCAL, D))
    return result.reshape(NI, D)
```

```python
import jax
import jax.numpy as jnp
from jax import lax
from jax.sharding import PartitionSpec as P

exponent_divisor = 0.03


def similar(query_factor, target_factor):
    return exponent_divisor * lax.dot_general(
        query_factor,
        target_factor,
        (((1,), (1,)), ((), ())),
        precision=lax.Precision.HIGHEST,
        preferred_element_type=jnp.float32,
    )


def rescaled_affinity(weights, features):
    return jnp.dot(
        weights, features, precision=lax.Precision.HIGHEST, preferred_element_type=jnp.float32
    )


def local(images, captions, bank):
    features = lax.all_gather(captions, "img", axis=1, tiled=True)
    querybank_similarity = similar(bank, features)
    local_peak = jnp.max(querybank_similarity, axis=0)
    local_total = jnp.sum(jnp.exp(querybank_similarity - local_peak[None, :]), axis=0)
    col_stats = lax.all_gather(jnp.stack([local_peak, local_total]), "img")
    raw = similar(images, features)
    peaks, totals = col_stats[:, 0], col_stats[:, 1]
    peak = jnp.max(peaks, axis=0)
    total = jnp.sum(totals * jnp.exp(peaks - peak[None, :]), axis=0)
    col_log = peak + jnp.log(total)
    logits = raw - col_log[None, :]
    row_peak = jnp.max(logits, axis=1)
    weights = jnp.exp(logits - row_peak[:, None])
    row_sum = jnp.sum(weights, axis=1)
    row_stats = lax.all_gather(jnp.stack([row_peak, row_sum]), "cap")
    summed = rescaled_affinity(weights, features)
    peaks, sums = row_stats[:, 0], row_stats[:, 1]
    top = jnp.max(peaks, axis=0)
    row_total = jnp.sum(sums * jnp.exp(peaks - top[None, :]), axis=0)
    summed = summed * jnp.exp(row_peak - top)[:, None]
    summed = lax.psum_scatter(summed, "cap", scatter_dimension=0, tiled=True)
    summed = lax.all_gather(summed, "cap", axis=0, tiled=True)
    return summed / row_total[:, None]


def solution(mesh):
    return jax.shard_map(
        local,
        mesh=mesh,
        in_specs=(P("img", None), P("cap", "img"), P("img", None)),
        out_specs=P("img", None),
        check_vma=False,
    )
```

```python
import jax
import jax.numpy as jnp
from jax import lax
from jax.sharding import Mesh
from jax.sharding import PartitionSpec as P

exponent_divisor = 0.03

IMG = ("zh", "y")
CAP = ("x", "zl", "core")


def similar(query_factor, target_factor):
    return exponent_divisor * lax.dot_general(
        query_factor,
        target_factor,
        (((1,), (1,)), ((), ())),
        precision=lax.Precision.HIGHEST,
        preferred_element_type=jnp.float32,
    )


def rescaled_affinity(weights, features):
    return jnp.dot(
        weights, features, precision=lax.Precision.HIGHEST, preferred_element_type=jnp.float32
    )


def merge_peaks(rounds, peak, total):
    pair = jnp.stack([peak, total])
    for axis, size, dist in rounds:
        other = lax.ppermute(pair, axis, [(j, j ^ dist) for j in range(size)])
        top = jnp.maximum(pair[0], other[0])
        both = pair[1] * jnp.exp(pair[0] - top) + other[1] * jnp.exp(other[0] - top)
        pair = jnp.stack([top, both])
    return pair[0], pair[1]


def local(images, captions, bank, sizes):
    img_rounds = [("zh", sizes["zh"], 1)] + [("y", sizes["y"], d) for d in (1, 2)]
    cap_rounds = [("core", sizes["core"], 1), ("zl", sizes["zl"], 1)] + [
        ("x", sizes["x"], d) for d in (1, 2)
    ]
    features = lax.all_gather(captions, IMG, axis=1, tiled=True)
    querybank_similarity = similar(bank, features)
    local_peak = jnp.max(querybank_similarity, axis=0)
    local_total = jnp.sum(jnp.exp(querybank_similarity - local_peak[None, :]), axis=0)
    raw = lax.optimization_barrier(similar(images, features))
    peak, total = merge_peaks(img_rounds, local_peak, local_total)
    col_log = peak + jnp.log(total)
    logits = raw - col_log[None, :]
    row_peak = jnp.max(logits, axis=1)
    weights = jnp.exp(logits - row_peak[:, None])
    row_sum = jnp.sum(weights, axis=1)
    summed = lax.optimization_barrier(rescaled_affinity(weights, features))
    top, row_total = merge_peaks(cap_rounds, row_peak, row_sum)
    summed = summed * jnp.exp(row_peak - top)[:, None]
    summed = lax.psum_scatter(summed, CAP, scatter_dimension=0, tiled=True)
    summed = lax.all_gather(summed, CAP, axis=0, tiled=True)
    return summed / row_total[:, None]


def solution(mesh):
    zh, y = 2, mesh.shape["img"] // 2
    zl, core = 2, 2
    x = mesh.shape["cap"] // (zl * core)
    sizes = dict(zh=zh, y=y, x=x, zl=zl, core=core)
    fine = Mesh(mesh.devices.reshape(zh, y, x, zl, core), ("zh", "y", "x", "zl", "core"))

    def run(images, captions, bank):
        return local(images, captions, bank, sizes)

    return jax.shard_map(
        run,
        mesh=fine,
        in_specs=(P(IMG, None), P(CAP, IMG), P(IMG, None)),
        out_specs=P(IMG, None),
        check_vma=False,
    )
```

```python
import jax
import jax.numpy as jnp
from jax import lax
from jax.sharding import Mesh
from jax.sharding import PartitionSpec as P

exponent_divisor = 0.03

IMG = ("zh", "y")
CAP = ("x", "zl", "core")


def similar(query_factor, target_factor):
    return exponent_divisor * lax.dot_general(
        query_factor,
        target_factor,
        (((1,), (1,)), ((), ())),
        precision=lax.Precision.HIGHEST,
        preferred_element_type=jnp.float32,
    )


def rescaled_affinity(weights, features):
    return jnp.dot(
        weights, features, precision=lax.Precision.HIGHEST, preferred_element_type=jnp.float32
    )


def merge_peaks(rounds, peak, total):
    pair = jnp.stack([peak, total])
    for axis, size, dist in rounds:
        other = lax.ppermute(pair, axis, [(j, j ^ dist) for j in range(size)])
        top = jnp.maximum(pair[0], other[0])
        both = pair[1] * jnp.exp(pair[0] - top) + other[1] * jnp.exp(other[0] - top)
        pair = jnp.stack([top, both])
    return pair[0], pair[1]


def ring(axis, size, step):
    return [(j, (j + step) % size) for j in range(size)]


def pick(stack, index):
    return lax.dynamic_index_in_dim(stack, index, axis=0, keepdims=False)


def reduce_rows(summed, row_total, offset, sizes):
    x_size = sizes["x"]
    c, p, z = lax.axis_index("core"), lax.axis_index("x"), lax.axis_index("zl")
    rows, width = summed.shape
    half = rows // 2
    piece = half // (2 * x_size)
    halves = summed.reshape(2, half, width)
    swap = [(0, 1), (1, 0)]
    held = pick(halves, c) + lax.ppermute(pick(halves, 1 - c), "core", swap)
    own = held.reshape(x_size, 2, piece, width)
    right, left = pick(own[:, 0], (p - 1) % x_size), pick(own[:, 1], (p + 1) % x_size)
    for s in range(x_size - 1):
        right = lax.ppermute(right, "x", ring("x", x_size, 1)) + pick(own[:, 0], (p - s - 2) % x_size)
        left = lax.ppermute(left, "x", ring("x", x_size, -1)) + pick(own[:, 1], (p + s + 2) % x_size)
    block = jnp.stack([right, left])
    mine = pick(block, z) + lax.ppermute(pick(block, 1 - z), "zl", swap)
    start = offset + c * half + p * (2 * piece) + z * piece
    mine = mine / lax.dynamic_slice_in_dim(row_total, start, piece)[:, None]
    other = lax.ppermute(mine, "zl", swap)
    block = jnp.where(z == 0, jnp.stack([mine, other]), jnp.stack([other, mine]))
    gathered = jnp.zeros((x_size, 2, piece, width), summed.dtype).at[p].set(block)
    right, left = block[0], block[1]
    for s in range(x_size - 1):
        right = lax.ppermute(right, "x", ring("x", x_size, 1))
        left = lax.ppermute(left, "x", ring("x", x_size, -1))
        gathered = gathered.at[(p - s - 1) % x_size, 0].set(right)
        gathered = gathered.at[(p + s + 1) % x_size, 1].set(left)
    held = gathered.reshape(half, width)
    other = lax.ppermute(held, "core", swap)
    return jnp.where(c == 0, jnp.stack([held, other]), jnp.stack([other, held])).reshape(rows, width)


def local(images, captions, bank, sizes):
    img_rounds = [("zh", sizes["zh"], 1)] + [("y", sizes["y"], d) for d in (1, 2)]
    cap_rounds = [("core", sizes["core"], 1), ("zl", sizes["zl"], 1)] + [
        ("x", sizes["x"], d) for d in (1, 2)
    ]
    features = lax.all_gather(captions, IMG, axis=1, tiled=True)
    querybank_similarity = similar(bank, features)
    local_peak = jnp.max(querybank_similarity, axis=0)
    local_total = jnp.sum(jnp.exp(querybank_similarity - local_peak[None, :]), axis=0)
    raw = lax.optimization_barrier(similar(images, features))
    peak, total = merge_peaks(img_rounds, local_peak, local_total)
    col_log = peak + jnp.log(total)
    logits = raw - col_log[None, :]
    row_peak = jnp.max(logits, axis=1)
    weights = jnp.exp(logits - row_peak[:, None])
    row_sum = jnp.sum(weights, axis=1)
    top, row_total = merge_peaks(cap_rounds, row_peak, row_sum)
    scale = jnp.exp(row_peak - top)
    rows = weights.shape[0]
    chunk = rows // 2
    parts = []
    for k in range(2):
        part = slice(k * chunk, (k + 1) * chunk)
        summed = rescaled_affinity(weights[part], features) * scale[part, None]
        parts.append(reduce_rows(summed, row_total, k * chunk, sizes))
    return jnp.concatenate(parts, axis=0)


def solution(mesh):
    zh, y = 2, mesh.shape["img"] // 2
    zl, core = 2, 2
    x = mesh.shape["cap"] // (zl * core)
    sizes = dict(zh=zh, y=y, x=x, zl=zl, core=core)
    fine = Mesh(mesh.devices.reshape(zh, y, x, zl, core), ("zh", "y", "x", "zl", "core"))

    def run(images, captions, bank):
        return local(images, captions, bank, sizes)

    return jax.shard_map(
        run,
        mesh=fine,
        in_specs=(P(IMG, None), P(CAP, IMG), P(IMG, None)),
        out_specs=P(IMG, None),
        check_vma=False,
    )
```

```python
import jax
import jax.numpy as jnp
from jax import lax
from jax.sharding import Mesh
from jax.sharding import PartitionSpec as P

exponent_divisor = 0.03

IMG = ("zh", "y")
CAP = ("x", "zl", "core")


def similar(query_factor, target_factor):
    return exponent_divisor * lax.dot_general(
        query_factor,
        target_factor,
        (((1,), (1,)), ((), ())),
        precision=lax.Precision.HIGHEST,
        preferred_element_type=jnp.float32,
    )


def rescaled_affinity(weights, features):
    return jnp.dot(
        weights, features, precision=lax.Precision.HIGHEST, preferred_element_type=jnp.float32
    )


def merge_peaks(rounds, peak, total):
    pair = jnp.stack([peak, total])
    for axis, size, dist in rounds:
        other = lax.ppermute(pair, axis, [(j, j ^ dist) for j in range(size)])
        top = jnp.maximum(pair[0], other[0])
        both = pair[1] * jnp.exp(pair[0] - top) + other[1] * jnp.exp(other[0] - top)
        pair = jnp.stack([top, both])
    return pair[0], pair[1]


def ring(axis, size, step):
    return [(j, (j + step) % size) for j in range(size)]


def pick(stack, index):
    return lax.dynamic_index_in_dim(stack, index, axis=0, keepdims=False)


def reduce_rows(summed, row_total, offset, sizes):
    x_size = sizes["x"]
    c, p, z = lax.axis_index("core"), lax.axis_index("x"), lax.axis_index("zl")
    rows, width = summed.shape
    half = rows // 2
    piece = half // (2 * x_size)
    halves = summed.reshape(2, half, width)
    swap = [(0, 1), (1, 0)]
    held = pick(halves, c) + lax.ppermute(pick(halves, 1 - c), "core", swap)
    own = held.reshape(x_size, 2, piece, width)
    right, left = pick(own[:, 0], (p - 1) % x_size), pick(own[:, 1], (p + 1) % x_size)
    for s in range(x_size - 1):
        right = lax.ppermute(right, "x", ring("x", x_size, 1)) + pick(own[:, 0], (p - s - 2) % x_size)
        left = lax.ppermute(left, "x", ring("x", x_size, -1)) + pick(own[:, 1], (p + s + 2) % x_size)
    block = jnp.stack([right, left])
    mine = pick(block, z) + lax.ppermute(pick(block, 1 - z), "zl", swap)
    start = offset + c * half + p * (2 * piece) + z * piece
    mine = mine / lax.dynamic_slice_in_dim(row_total, start, piece)[:, None]
    other = lax.ppermute(mine, "zl", swap)
    block = jnp.where(z == 0, jnp.stack([mine, other]), jnp.stack([other, mine]))
    gathered = jnp.zeros((x_size, 2, piece, width), summed.dtype).at[p].set(block)
    right, left = block[0], block[1]
    for s in range(x_size - 1):
        right = lax.ppermute(right, "x", ring("x", x_size, 1))
        left = lax.ppermute(left, "x", ring("x", x_size, -1))
        gathered = gathered.at[(p - s - 1) % x_size, 0].set(right)
        gathered = gathered.at[(p + s + 1) % x_size, 1].set(left)
    held = gathered.reshape(half, width)
    other = lax.ppermute(held, "core", swap)
    return jnp.where(c == 0, jnp.stack([held, other]), jnp.stack([other, held])).reshape(rows, width)


def gather_features(captions, sizes):
    y_size = sizes["y"]
    rows, width = captions.shape
    half = rows // 2
    offloaded = lax.all_gather(captions[:half], IMG, axis=1, tiled=True)
    mine = captions[half:]
    h, y = lax.axis_index("zh"), lax.axis_index("y")
    other = lax.ppermute(mine, "zh", [(0, 1), (1, 0)])
    pair = jnp.where(h == 0, jnp.stack([mine, other]), jnp.stack([other, mine]))
    got = jnp.zeros((y_size, 2, half, width), captions.dtype).at[y].set(pair)
    right, left = pair[0], pair[1]
    for s in range(y_size - 1):
        right = lax.ppermute(right, "y", ring("y", y_size, 1))
        left = lax.ppermute(left, "y", ring("y", y_size, -1))
        got = got.at[(y - s - 1) % y_size, 0].set(right)
        got = got.at[(y + s + 1) % y_size, 1].set(left)
    ringed = got.transpose(2, 1, 0, 3).reshape(half, 2 * y_size * width)
    return jnp.concatenate([offloaded, ringed], axis=0)


def local(images, captions, bank, sizes):
    img_rounds = [("zh", sizes["zh"], 1)] + [("y", sizes["y"], d) for d in (1, 2)]
    cap_rounds = [("core", sizes["core"], 1), ("zl", sizes["zl"], 1)] + [
        ("x", sizes["x"], d) for d in (1, 2)
    ]
    features = gather_features(captions, sizes)
    querybank_similarity = similar(bank, features)
    local_peak = jnp.max(querybank_similarity, axis=0)
    local_total = jnp.sum(jnp.exp(querybank_similarity - local_peak[None, :]), axis=0)
    raw = lax.optimization_barrier(similar(images, features))
    peak, total = merge_peaks(img_rounds, local_peak, local_total)
    col_log = peak + jnp.log(total)
    logits = raw - col_log[None, :]
    row_peak = jnp.max(logits, axis=1)
    weights = jnp.exp(logits - row_peak[:, None])
    row_sum = jnp.sum(weights, axis=1)
    top, row_total = merge_peaks(cap_rounds, row_peak, row_sum)
    scale = jnp.exp(row_peak - top)
    rows = weights.shape[0]
    chunk = rows // 2
    parts = []
    for k in range(2):
        part = slice(k * chunk, (k + 1) * chunk)
        summed = rescaled_affinity(weights[part], features) * scale[part, None]
        parts.append(reduce_rows(summed, row_total, k * chunk, sizes))
    return jnp.concatenate(parts, axis=0)


def solution(mesh):
    zh, y = 2, mesh.shape["img"] // 2
    zl, core = 2, 2
    x = mesh.shape["cap"] // (zl * core)
    sizes = dict(zh=zh, y=y, x=x, zl=zl, core=core)
    fine = Mesh(mesh.devices.reshape(zh, y, x, zl, core), ("zh", "y", "x", "zl", "core"))

    def run(images, captions, bank):
        return local(images, captions, bank, sizes)

    return jax.shard_map(
        run,
        mesh=fine,
        in_specs=(P(IMG, None), P(CAP, IMG), P(IMG, None)),
        out_specs=P(IMG, None),
        check_vma=False,
    )
```

```python
import jax
import jax.numpy as jnp
from jax import lax
from jax.sharding import Mesh
from jax.sharding import PartitionSpec as P

exponent_divisor = 0.03

IMG = ("zh", "y")
CAP = ("x", "zl", "core")


def similar(query_factor, target_factor):
    return exponent_divisor * lax.dot_general(
        query_factor,
        target_factor,
        (((1,), (1,)), ((), ())),
        precision=lax.Precision.HIGHEST,
        preferred_element_type=jnp.float32,
    )


def rescaled_affinity(weights, features):
    return jnp.dot(
        weights, features, precision=lax.Precision.HIGHEST, preferred_element_type=jnp.float32
    )


def merge_peaks(rounds, peak, total):
    pair = jnp.stack([peak, total])
    for axis, size, dist in rounds:
        other = lax.ppermute(pair, axis, [(j, j ^ dist) for j in range(size)])
        top = jnp.maximum(pair[0], other[0])
        both = pair[1] * jnp.exp(pair[0] - top) + other[1] * jnp.exp(other[0] - top)
        pair = jnp.stack([top, both])
    return pair[0], pair[1]


def ring(axis, size, step):
    return [(j, (j + step) % size) for j in range(size)]


def pick(stack, index):
    return lax.dynamic_index_in_dim(stack, index, axis=0, keepdims=False)


def reduce_rows(summed, row_total, offset, sizes):
    x_size = sizes["x"]
    c, p, z = lax.axis_index("core"), lax.axis_index("x"), lax.axis_index("zl")
    rows, width = summed.shape
    half = rows // 2
    piece = half // (2 * x_size)
    halves = summed.reshape(2, half, width)
    swap = [(0, 1), (1, 0)]
    held = pick(halves, c) + lax.ppermute(pick(halves, 1 - c), "core", swap)
    own = held.reshape(x_size, 2, piece, width)
    right, left = pick(own[:, 0], (p - 1) % x_size), pick(own[:, 1], (p + 1) % x_size)
    for s in range(x_size - 1):
        right = lax.ppermute(right, "x", ring("x", x_size, 1)) + pick(own[:, 0], (p - s - 2) % x_size)
        left = lax.ppermute(left, "x", ring("x", x_size, -1)) + pick(own[:, 1], (p + s + 2) % x_size)
    block = jnp.stack([right, left])
    mine = pick(block, z) + lax.ppermute(pick(block, 1 - z), "zl", swap)
    start = offset + c * half + p * (2 * piece) + z * piece
    mine = mine / lax.dynamic_slice_in_dim(row_total, start, piece)[:, None]
    other = lax.ppermute(mine, "zl", swap)
    block = jnp.where(z == 0, jnp.stack([mine, other]), jnp.stack([other, mine]))
    gathered = jnp.zeros((x_size, 2, piece, width), summed.dtype).at[p].set(block)
    right, left = block[0], block[1]
    for s in range(x_size - 1):
        right = lax.ppermute(right, "x", ring("x", x_size, 1))
        left = lax.ppermute(left, "x", ring("x", x_size, -1))
        gathered = gathered.at[(p - s - 1) % x_size, 0].set(right)
        gathered = gathered.at[(p + s + 1) % x_size, 1].set(left)
    held = gathered.reshape(half, width)
    other = lax.ppermute(held, "core", swap)
    return jnp.where(c == 0, jnp.stack([held, other]), jnp.stack([other, held])).reshape(rows, width)


def gather_features(captions, sizes):
    y_size = sizes["y"]
    rows, width = captions.shape
    half = rows // 2
    offloaded = lax.all_gather(captions[:half], IMG, axis=1, tiled=True)
    mine = captions[half:]
    h, y = lax.axis_index("zh"), lax.axis_index("y")
    other = lax.ppermute(mine, "zh", [(0, 1), (1, 0)])
    pair = jnp.where(h == 0, jnp.stack([mine, other]), jnp.stack([other, mine]))
    got = jnp.zeros((y_size, 2, half, width), captions.dtype).at[y].set(pair)
    right, left = pair[0], pair[1]
    for s in range(y_size - 1):
        right = lax.ppermute(right, "y", ring("y", y_size, 1))
        left = lax.ppermute(left, "y", ring("y", y_size, -1))
        got = got.at[(y - s - 1) % y_size, 0].set(right)
        got = got.at[(y + s + 1) % y_size, 1].set(left)
    ringed = got.transpose(2, 1, 0, 3).reshape(half, 2 * y_size * width)
    return lax.optimization_barrier(jnp.concatenate([offloaded, ringed], axis=0))


def local(images, captions, bank, sizes):
    img_rounds = [("zh", sizes["zh"], 1)] + [("y", sizes["y"], d) for d in (1, 2)]
    cap_rounds = [("core", sizes["core"], 1), ("zl", sizes["zl"], 1)] + [
        ("x", sizes["x"], d) for d in (1, 2)
    ]
    features = gather_features(captions, sizes)
    querybank_similarity = similar(bank, features)
    local_peak = jnp.max(querybank_similarity, axis=0)
    local_total = jnp.sum(jnp.exp(querybank_similarity - local_peak[None, :]), axis=0)
    raw = lax.optimization_barrier(similar(images, features))
    peak, total = merge_peaks(img_rounds, local_peak, local_total)
    col_log = peak + jnp.log(total)
    logits = raw - col_log[None, :]
    row_peak = jnp.max(logits, axis=1)
    weights = jnp.exp(logits - row_peak[:, None])
    row_sum = jnp.sum(weights, axis=1)
    top, row_total = merge_peaks(cap_rounds, row_peak, row_sum)
    scale = jnp.exp(row_peak - top)
    rows = weights.shape[0]
    chunk = rows // 2
    parts = []
    for k in range(2):
        part = slice(k * chunk, (k + 1) * chunk)
        summed = rescaled_affinity(weights[part], features) * scale[part, None]
        parts.append(reduce_rows(summed, row_total, k * chunk, sizes))
    return jnp.concatenate(parts, axis=0)


def solution(mesh):
    zh, y = 2, mesh.shape["img"] // 2
    zl, core = 2, 2
    x = mesh.shape["cap"] // (zl * core)
    sizes = dict(zh=zh, y=y, x=x, zl=zl, core=core)
    fine = Mesh(mesh.devices.reshape(zh, y, x, zl, core), ("zh", "y", "x", "zl", "core"))

    def run(images, captions, bank):
        return local(images, captions, bank, sizes)

    return jax.shard_map(
        run,
        mesh=fine,
        in_specs=(P(IMG, None), P(CAP, IMG), P(IMG, None)),
        out_specs=P(IMG, None),
        check_vma=False,
    )
```

```python
import jax
import jax.numpy as jnp
from jax import lax
from jax.sharding import Mesh
from jax.sharding import PartitionSpec as P

exponent_divisor = 0.03

IMG = ("zh", "y")
CAP = ("x", "zl", "core")
ORDERS = (("core", "x", "zl"), ("core", "zl", "x"))


def similar(query_factor, target_factor):
    return exponent_divisor * lax.dot_general(
        query_factor,
        target_factor,
        (((1,), (1,)), ((), ())),
        precision=lax.Precision.HIGHEST,
        preferred_element_type=jnp.float32,
    )


def rescaled_affinity(weights, features):
    return jnp.dot(
        weights, features, precision=lax.Precision.HIGHEST, preferred_element_type=jnp.float32
    )


def merge_peaks(rounds, peak, total):
    pair = jnp.stack([peak, total])
    for axis, size, dist in rounds:
        other = lax.ppermute(pair, axis, [(j, j ^ dist) for j in range(size)])
        top = jnp.maximum(pair[0], other[0])
        both = pair[1] * jnp.exp(pair[0] - top) + other[1] * jnp.exp(other[0] - top)
        pair = jnp.stack([top, both])
    return pair[0], pair[1]


def ring(axis, size, step):
    return [(j, (j + step) % size) for j in range(size)]


def pick(stack, index):
    return lax.dynamic_index_in_dim(stack, index, axis=0, keepdims=False)


def scatter_stage(data, axis, size):
    q = lax.axis_index(axis)
    rows, width = data.shape
    if size == 2:
        halves = data.reshape(2, rows // 2, width)
        return pick(halves, q) + lax.ppermute(pick(halves, 1 - q), axis, [(0, 1), (1, 0)])
    piece = rows // (2 * size)
    own = data.reshape(size, 2, piece, width)
    right, left = pick(own[:, 0], (q - 1) % size), pick(own[:, 1], (q + 1) % size)
    for s in range(size - 1):
        right = lax.ppermute(right, axis, ring(axis, size, 1)) + pick(own[:, 0], (q - s - 2) % size)
        left = lax.ppermute(left, axis, ring(axis, size, -1)) + pick(own[:, 1], (q + s + 2) % size)
    return jnp.concatenate([right, left], axis=0)


def gather_stage(data, axis, size):
    q = lax.axis_index(axis)
    rows, width = data.shape
    if size == 2:
        other = lax.ppermute(data, axis, [(0, 1), (1, 0)])
        both = jnp.where(q == 0, jnp.stack([data, other]), jnp.stack([other, data]))
        return both.reshape(2 * rows, width)
    piece = rows // 2
    block = data.reshape(2, piece, width)
    gathered = jnp.zeros((size, 2, piece, width), data.dtype).at[q].set(block)
    right, left = block[0], block[1]
    for s in range(size - 1):
        right = lax.ppermute(right, axis, ring(axis, size, 1))
        left = lax.ppermute(left, axis, ring(axis, size, -1))
        gathered = gathered.at[(q - s - 1) % size, 0].set(right)
        gathered = gathered.at[(q + s + 1) % size, 1].set(left)
    return gathered.reshape(size * rows, width)


def reduce_rows(summed, row_total, offset, sizes, order):
    data, start = summed, offset
    for axis in order:
        data = scatter_stage(data, axis, sizes[axis])
        start = start + lax.axis_index(axis) * data.shape[0]
    data = data / lax.dynamic_slice_in_dim(row_total, start, data.shape[0])[:, None]
    for axis in reversed(order):
        data = gather_stage(data, axis, sizes[axis])
    return data


def local(images, captions, bank, sizes):
    img_rounds = [("zh", sizes["zh"], 1)] + [("y", sizes["y"], d) for d in (1, 2)]
    cap_rounds = [("core", sizes["core"], 1), ("zl", sizes["zl"], 1)] + [
        ("x", sizes["x"], d) for d in (1, 2)
    ]
    features = lax.all_gather(captions, IMG, axis=1, tiled=True)
    querybank_similarity = similar(bank, features)
    local_peak = jnp.max(querybank_similarity, axis=0)
    local_total = jnp.sum(jnp.exp(querybank_similarity - local_peak[None, :]), axis=0)
    raw = lax.optimization_barrier(similar(images, features))
    peak, total = merge_peaks(img_rounds, local_peak, local_total)
    col_log = peak + jnp.log(total)
    logits = raw - col_log[None, :]
    row_peak = jnp.max(logits, axis=1)
    weights = jnp.exp(logits - row_peak[:, None])
    row_sum = jnp.sum(weights, axis=1)
    top, row_total = merge_peaks(cap_rounds, row_peak, row_sum)
    scale = jnp.exp(row_peak - top)
    rows = weights.shape[0]
    chunk = rows // 2
    parts = []
    for k in range(2):
        part = slice(k * chunk, (k + 1) * chunk)
        summed = rescaled_affinity(weights[part], features) * scale[part, None]
        parts.append(reduce_rows(summed, row_total, k * chunk, sizes, ORDERS[k]))
    return jnp.concatenate(parts, axis=0)


def solution(mesh):
    zh, y = 2, mesh.shape["img"] // 2
    zl, core = 2, 2
    x = mesh.shape["cap"] // (zl * core)
    sizes = dict(zh=zh, y=y, x=x, zl=zl, core=core)
    fine = Mesh(mesh.devices.reshape(zh, y, x, zl, core), ("zh", "y", "x", "zl", "core"))

    def run(images, captions, bank):
        return local(images, captions, bank, sizes)

    return jax.shard_map(
        run,
        mesh=fine,
        in_specs=(P(IMG, None), P(CAP, IMG), P(IMG, None)),
        out_specs=P(IMG, None),
        check_vma=False,
    )
```

```python
import jax
import jax.numpy as jnp
from jax import lax
from jax.experimental.layout import Layout, with_layout_constraint
from jax.sharding import Mesh
from jax.sharding import PartitionSpec as P

exponent_divisor = 0.03

IMG = ("zh", "y")
CAP = ("x", "zl", "core")


def similar(query_factor, target_factor):
    product = lax.dot_general(
        query_factor,
        target_factor,
        (((1,), (0,)), ((), ())),
        precision=lax.Precision.HIGHEST,
        preferred_element_type=jnp.float32,
    )
    return exponent_divisor * with_layout_constraint(product, Layout((0, 1)))


def rescaled_affinity(weights, features):
    return lax.dot_general(
        weights,
        features,
        (((1,), (1,)), ((), ())),
        precision=lax.Precision.HIGHEST,
        preferred_element_type=jnp.float32,
    )


def merge_peaks(rounds, peak, total):
    pair = jnp.stack([peak, total])
    for axis, size, dist in rounds:
        other = lax.ppermute(pair, axis, [(j, j ^ dist) for j in range(size)])
        top = jnp.maximum(pair[0], other[0])
        both = pair[1] * jnp.exp(pair[0] - top) + other[1] * jnp.exp(other[0] - top)
        pair = jnp.stack([top, both])
    return pair[0], pair[1]


def ring(axis, size, step):
    return [(j, (j + step) % size) for j in range(size)]


def pick(stack, index):
    return lax.dynamic_index_in_dim(stack, index, axis=0, keepdims=False)


def reduce_rows(summed, row_total, offset, sizes):
    x_size = sizes["x"]
    c, p, z = lax.axis_index("core"), lax.axis_index("x"), lax.axis_index("zl")
    rows, width = summed.shape
    half = rows // 2
    piece = half // (2 * x_size)
    halves = summed.reshape(2, half, width)
    swap = [(0, 1), (1, 0)]
    held = pick(halves, c) + lax.ppermute(pick(halves, 1 - c), "core", swap)
    own = held.reshape(x_size, 2, piece, width)
    right, left = pick(own[:, 0], (p - 1) % x_size), pick(own[:, 1], (p + 1) % x_size)
    for s in range(x_size - 1):
        right = lax.ppermute(right, "x", ring("x", x_size, 1)) + pick(own[:, 0], (p - s - 2) % x_size)
        left = lax.ppermute(left, "x", ring("x", x_size, -1)) + pick(own[:, 1], (p + s + 2) % x_size)
    block = jnp.stack([right, left])
    mine = pick(block, z) + lax.ppermute(pick(block, 1 - z), "zl", swap)
    start = offset + c * half + p * (2 * piece) + z * piece
    mine = mine / lax.dynamic_slice_in_dim(row_total, start, piece)[:, None]
    other = lax.ppermute(mine, "zl", swap)
    block = jnp.where(z == 0, jnp.stack([mine, other]), jnp.stack([other, mine]))
    gathered = jnp.zeros((x_size, 2, piece, width), summed.dtype).at[p].set(block)
    right, left = block[0], block[1]
    for s in range(x_size - 1):
        right = lax.ppermute(right, "x", ring("x", x_size, 1))
        left = lax.ppermute(left, "x", ring("x", x_size, -1))
        gathered = gathered.at[(p - s - 1) % x_size, 0].set(right)
        gathered = gathered.at[(p + s + 1) % x_size, 1].set(left)
    held = gathered.reshape(half, width)
    other = lax.ppermute(held, "core", swap)
    return jnp.where(c == 0, jnp.stack([held, other]), jnp.stack([other, held])).reshape(rows, width)


def gather_features(captions, sizes):
    y_size = sizes["y"]
    rows, width = captions.shape
    h, y = lax.axis_index("zh"), lax.axis_index("y")
    other = lax.ppermute(captions, "zh", [(0, 1), (1, 0)])
    pair = jnp.where(h == 0, jnp.stack([captions, other]), jnp.stack([other, captions]))
    got = jnp.zeros((y_size, 2, rows, width), captions.dtype).at[y].set(pair)
    right, left = pair[0], pair[1]
    for s in range(y_size - 1):
        right = lax.ppermute(right, "y", ring("y", y_size, 1))
        left = lax.ppermute(left, "y", ring("y", y_size, -1))
        got = got.at[(y - s - 1) % y_size, 0].set(right)
        got = got.at[(y + s + 1) % y_size, 1].set(left)
    return got.transpose(1, 0, 3, 2).reshape(2 * y_size * width, rows)


def local(images, captions, bank, sizes):
    img_rounds = [("zh", sizes["zh"], 1)] + [("y", sizes["y"], d) for d in (1, 2)]
    cap_rounds = [("core", sizes["core"], 1), ("zl", sizes["zl"], 1)] + [
        ("x", sizes["x"], d) for d in (1, 2)
    ]
    features = gather_features(captions, sizes)
    querybank_similarity = similar(bank, features)
    local_peak = jnp.max(querybank_similarity, axis=0)
    local_total = jnp.sum(jnp.exp(querybank_similarity - local_peak[None, :]), axis=0)
    raw = lax.optimization_barrier(similar(images, features))
    peak, total = merge_peaks(img_rounds, local_peak, local_total)
    col_log = peak + jnp.log(total)
    logits = raw - col_log[None, :]
    row_peak = jnp.max(logits, axis=1)
    weights = jnp.exp(logits - row_peak[:, None])
    row_sum = jnp.sum(weights, axis=1)
    top, row_total = merge_peaks(cap_rounds, row_peak, row_sum)
    scale = jnp.exp(row_peak - top)
    rows = weights.shape[0]
    chunk = rows // 2
    parts = []
    for k in range(2):
        part = slice(k * chunk, (k + 1) * chunk)
        summed = rescaled_affinity(weights[part], features) * scale[part, None]
        parts.append(reduce_rows(summed, row_total, k * chunk, sizes))
    return jnp.concatenate(parts, axis=0)


def solution(mesh):
    zh, y = 2, mesh.shape["img"] // 2
    zl, core = 2, 2
    x = mesh.shape["cap"] // (zl * core)
    sizes = dict(zh=zh, y=y, x=x, zl=zl, core=core)
    fine = Mesh(mesh.devices.reshape(zh, y, x, zl, core), ("zh", "y", "x", "zl", "core"))

    def run(images, captions, bank):
        return local(images, captions, bank, sizes)

    return jax.shard_map(
        run,
        mesh=fine,
        in_specs=(P(IMG, None), P(CAP, IMG), P(IMG, None)),
        out_specs=P(IMG, None),
        check_vma=False,
    )
```

```python
import jax
import jax.numpy as jnp
from jax import lax
from jax.experimental.layout import Layout, with_layout_constraint
from jax.sharding import Mesh
from jax.sharding import PartitionSpec as P

exponent_divisor = 0.03

IMG = ("zh", "y")
CAP = ("x", "zl", "core")
CHUNKS = 1


def similar(query_factor, target_factor):
    product = lax.dot_general(
        query_factor,
        target_factor,
        (((1,), (0,)), ((), ())),
        precision=lax.Precision.HIGHEST,
        preferred_element_type=jnp.float32,
    )
    return exponent_divisor * with_layout_constraint(product, Layout((0, 1)))


def rescaled_affinity(weights, features):
    return lax.dot_general(
        weights,
        features,
        (((1,), (1,)), ((), ())),
        precision=lax.Precision.HIGHEST,
        preferred_element_type=jnp.float32,
    )


def merge_peaks(rounds, peak, total):
    pair = jnp.stack([peak, total])
    for axis, size, dist in rounds:
        other = lax.ppermute(pair, axis, [(j, j ^ dist) for j in range(size)])
        top = jnp.maximum(pair[0], other[0])
        both = pair[1] * jnp.exp(pair[0] - top) + other[1] * jnp.exp(other[0] - top)
        pair = jnp.stack([top, both])
    return pair[0], pair[1]


def ring(axis, size, step):
    return [(j, (j + step) % size) for j in range(size)]


def pick(stack, index):
    return lax.dynamic_index_in_dim(stack, index, axis=0, keepdims=False)


def reduce_rows(summed, row_total, offset, sizes):
    x_size = sizes["x"]
    c, p, z = lax.axis_index("core"), lax.axis_index("x"), lax.axis_index("zl")
    rows, width = summed.shape
    half = rows // 2
    piece = half // (2 * x_size)
    halves = summed.reshape(2, half, width)
    swap = [(0, 1), (1, 0)]
    held = pick(halves, c) + lax.ppermute(pick(halves, 1 - c), "core", swap)
    own = held.reshape(x_size, 2, piece, width)
    right, left = pick(own[:, 0], (p - 1) % x_size), pick(own[:, 1], (p + 1) % x_size)
    for s in range(x_size - 1):
        right = lax.ppermute(right, "x", ring("x", x_size, 1)) + pick(own[:, 0], (p - s - 2) % x_size)
        left = lax.ppermute(left, "x", ring("x", x_size, -1)) + pick(own[:, 1], (p + s + 2) % x_size)
    block = jnp.stack([right, left])
    mine = pick(block, z) + lax.ppermute(pick(block, 1 - z), "zl", swap)
    start = offset + c * half + p * (2 * piece) + z * piece
    mine = mine / lax.dynamic_slice_in_dim(row_total, start, piece)[:, None]
    other = lax.ppermute(mine, "zl", swap)
    block = jnp.where(z == 0, jnp.stack([mine, other]), jnp.stack([other, mine]))
    gathered = jnp.zeros((x_size, 2, piece, width), summed.dtype).at[p].set(block)
    right, left = block[0], block[1]
    for s in range(x_size - 1):
        right = lax.ppermute(right, "x", ring("x", x_size, 1))
        left = lax.ppermute(left, "x", ring("x", x_size, -1))
        gathered = gathered.at[(p - s - 1) % x_size, 0].set(right)
        gathered = gathered.at[(p + s + 1) % x_size, 1].set(left)
    held = gathered.reshape(half, width)
    other = lax.ppermute(held, "core", swap)
    return jnp.where(c == 0, jnp.stack([held, other]), jnp.stack([other, held])).reshape(rows, width)


def gather_features(captions, sizes):
    y_size = sizes["y"]
    rows, width = captions.shape
    h, y = lax.axis_index("zh"), lax.axis_index("y")
    other = lax.ppermute(captions, "zh", [(0, 1), (1, 0)])
    pair = jnp.where(h == 0, jnp.stack([captions, other]), jnp.stack([other, captions]))
    got = jnp.zeros((y_size, 2, rows, width), captions.dtype).at[y].set(pair)
    right, left = pair[0], pair[1]
    for s in range(y_size - 1):
        right = lax.ppermute(right, "y", ring("y", y_size, 1))
        left = lax.ppermute(left, "y", ring("y", y_size, -1))
        got = got.at[(y - s - 1) % y_size, 0].set(right)
        got = got.at[(y + s + 1) % y_size, 1].set(left)
    return got.transpose(1, 0, 3, 2).reshape(2 * y_size * width, rows)


def local(images, captions, bank, sizes):
    img_rounds = [("zh", sizes["zh"], 1)] + [("y", sizes["y"], d) for d in (1, 2)]
    cap_rounds = [("core", sizes["core"], 1), ("zl", sizes["zl"], 1)] + [
        ("x", sizes["x"], d) for d in (1, 2)
    ]
    features = gather_features(captions, sizes)
    querybank_similarity = similar(bank, features)
    local_peak = jnp.max(querybank_similarity, axis=0)
    local_total = jnp.sum(jnp.exp(querybank_similarity - local_peak[None, :]), axis=0)
    raw = lax.optimization_barrier(similar(images, features))
    peak, total = merge_peaks(img_rounds, local_peak, local_total)
    col_log = peak + jnp.log(total)
    logits = raw - col_log[None, :]
    row_peak = jnp.max(logits, axis=1)
    weights = jnp.exp(logits - row_peak[:, None])
    row_sum = jnp.sum(weights, axis=1)
    top, row_total = merge_peaks(cap_rounds, row_peak, row_sum)
    scale = jnp.exp(row_peak - top)
    rows = weights.shape[0]
    chunk = rows // CHUNKS
    parts = []
    for k in range(CHUNKS):
        part = slice(k * chunk, (k + 1) * chunk)
        summed = rescaled_affinity(weights[part], features) * scale[part, None]
        parts.append(reduce_rows(summed, row_total, k * chunk, sizes))
    return jnp.concatenate(parts, axis=0)


def solution(mesh):
    zh, y = 2, mesh.shape["img"] // 2
    zl, core = 2, 2
    x = mesh.shape["cap"] // (zl * core)
    sizes = dict(zh=zh, y=y, x=x, zl=zl, core=core)
    fine = Mesh(mesh.devices.reshape(zh, y, x, zl, core), ("zh", "y", "x", "zl", "core"))

    def run(images, captions, bank):
        return local(images, captions, bank, sizes)

    return jax.shard_map(
        run,
        mesh=fine,
        in_specs=(P(IMG, None), P(CAP, IMG), P(IMG, None)),
        out_specs=P(IMG, None),
        check_vma=False,
    )
```

```python
import jax
import jax.numpy as jnp
from jax import lax
from jax.experimental.layout import Layout, with_layout_constraint
from jax.sharding import Mesh
from jax.sharding import PartitionSpec as P

exponent_divisor = 0.03

IMG = ("zh", "y")
CAP = ("x", "zl", "core")
CHUNKS = 4


def similar(query_factor, target_factor):
    product = lax.dot_general(
        query_factor,
        target_factor,
        (((1,), (0,)), ((), ())),
        precision=lax.Precision.HIGHEST,
        preferred_element_type=jnp.float32,
    )
    return exponent_divisor * with_layout_constraint(product, Layout((0, 1)))


def rescaled_affinity(weights, features):
    return lax.dot_general(
        weights,
        features,
        (((1,), (1,)), ((), ())),
        precision=lax.Precision.HIGHEST,
        preferred_element_type=jnp.float32,
    )


def merge_peaks(rounds, peak, total):
    pair = jnp.stack([peak, total])
    for axis, size, dist in rounds:
        other = lax.ppermute(pair, axis, [(j, j ^ dist) for j in range(size)])
        top = jnp.maximum(pair[0], other[0])
        both = pair[1] * jnp.exp(pair[0] - top) + other[1] * jnp.exp(other[0] - top)
        pair = jnp.stack([top, both])
    return pair[0], pair[1]


def ring(axis, size, step):
    return [(j, (j + step) % size) for j in range(size)]


def pick(stack, index):
    return lax.dynamic_index_in_dim(stack, index, axis=0, keepdims=False)


def reduce_rows(summed, row_total, offset, sizes):
    x_size = sizes["x"]
    c, p, z = lax.axis_index("core"), lax.axis_index("x"), lax.axis_index("zl")
    rows, width = summed.shape
    half = rows // 2
    piece = half // (2 * x_size)
    halves = summed.reshape(2, half, width)
    swap = [(0, 1), (1, 0)]
    held = pick(halves, c) + lax.ppermute(pick(halves, 1 - c), "core", swap)
    own = held.reshape(x_size, 2, piece, width)
    right, left = pick(own[:, 0], (p - 1) % x_size), pick(own[:, 1], (p + 1) % x_size)
    for s in range(x_size - 1):
        right = lax.ppermute(right, "x", ring("x", x_size, 1)) + pick(own[:, 0], (p - s - 2) % x_size)
        left = lax.ppermute(left, "x", ring("x", x_size, -1)) + pick(own[:, 1], (p + s + 2) % x_size)
    block = jnp.stack([right, left])
    mine = pick(block, z) + lax.ppermute(pick(block, 1 - z), "zl", swap)
    start = offset + c * half + p * (2 * piece) + z * piece
    mine = mine / lax.dynamic_slice_in_dim(row_total, start, piece)[:, None]
    other = lax.ppermute(mine, "zl", swap)
    block = jnp.where(z == 0, jnp.stack([mine, other]), jnp.stack([other, mine]))
    gathered = jnp.zeros((x_size, 2, piece, width), summed.dtype).at[p].set(block)
    right, left = block[0], block[1]
    for s in range(x_size - 1):
        right = lax.ppermute(right, "x", ring("x", x_size, 1))
        left = lax.ppermute(left, "x", ring("x", x_size, -1))
        gathered = gathered.at[(p - s - 1) % x_size, 0].set(right)
        gathered = gathered.at[(p + s + 1) % x_size, 1].set(left)
    held = gathered.reshape(half, width)
    other = lax.ppermute(held, "core", swap)
    return jnp.where(c == 0, jnp.stack([held, other]), jnp.stack([other, held])).reshape(rows, width)


def gather_features(captions, sizes):
    y_size = sizes["y"]
    rows, width = captions.shape
    h, y = lax.axis_index("zh"), lax.axis_index("y")
    other = lax.ppermute(captions, "zh", [(0, 1), (1, 0)])
    pair = jnp.where(h == 0, jnp.stack([captions, other]), jnp.stack([other, captions]))
    got = jnp.zeros((y_size, 2, rows, width), captions.dtype).at[y].set(pair)
    right, left = pair[0], pair[1]
    for s in range(y_size - 1):
        right = lax.ppermute(right, "y", ring("y", y_size, 1))
        left = lax.ppermute(left, "y", ring("y", y_size, -1))
        got = got.at[(y - s - 1) % y_size, 0].set(right)
        got = got.at[(y + s + 1) % y_size, 1].set(left)
    return got.transpose(1, 0, 3, 2).reshape(2 * y_size * width, rows)


def local(images, captions, bank, sizes):
    img_rounds = [("zh", sizes["zh"], 1)] + [("y", sizes["y"], d) for d in (1, 2)]
    cap_rounds = [("core", sizes["core"], 1), ("zl", sizes["zl"], 1)] + [
        ("x", sizes["x"], d) for d in (1, 2)
    ]
    features = gather_features(captions, sizes)
    querybank_similarity = similar(bank, features)
    local_peak = jnp.max(querybank_similarity, axis=0)
    local_total = jnp.sum(jnp.exp(querybank_similarity - local_peak[None, :]), axis=0)
    raw = lax.optimization_barrier(similar(images, features))
    peak, total = merge_peaks(img_rounds, local_peak, local_total)
    col_log = peak + jnp.log(total)
    logits = raw - col_log[None, :]
    row_peak = jnp.max(logits, axis=1)
    weights = jnp.exp(logits - row_peak[:, None])
    row_sum = jnp.sum(weights, axis=1)
    top, row_total = merge_peaks(cap_rounds, row_peak, row_sum)
    scale = jnp.exp(row_peak - top)
    rows = weights.shape[0]
    chunk = rows // CHUNKS
    parts = []
    for k in range(CHUNKS):
        part = slice(k * chunk, (k + 1) * chunk)
        summed = rescaled_affinity(weights[part], features) * scale[part, None]
        parts.append(reduce_rows(summed, row_total, k * chunk, sizes))
    return jnp.concatenate(parts, axis=0)


def solution(mesh):
    zh, y = 2, mesh.shape["img"] // 2
    zl, core = 2, 2
    x = mesh.shape["cap"] // (zl * core)
    sizes = dict(zh=zh, y=y, x=x, zl=zl, core=core)
    fine = Mesh(mesh.devices.reshape(zh, y, x, zl, core), ("zh", "y", "x", "zl", "core"))

    def run(images, captions, bank):
        return local(images, captions, bank, sizes)

    return jax.shard_map(
        run,
        mesh=fine,
        in_specs=(P(IMG, None), P(CAP, IMG), P(IMG, None)),
        out_specs=P(IMG, None),
        check_vma=False,
    )
```

```python
import jax
import jax.numpy as jnp
from jax import lax
from jax.experimental.layout import Layout, with_layout_constraint
from jax.sharding import Mesh
from jax.sharding import PartitionSpec as P

exponent_divisor = 0.03

IMG = ("zh", "y")
CAP = ("x", "zl", "core")


def similar(query_factor, target_factor):
    product = lax.dot_general(
        query_factor,
        target_factor,
        (((1,), (0,)), ((), ())),
        precision=lax.Precision.HIGHEST,
        preferred_element_type=jnp.float32,
    )
    return exponent_divisor * with_layout_constraint(product, Layout((0, 1)))


def rescaled_affinity(weights, features):
    return lax.dot_general(
        weights,
        features,
        (((1,), (1,)), ((), ())),
        precision=lax.Precision.HIGHEST,
        preferred_element_type=jnp.float32,
    )


def merge_peaks(rounds, peak, total):
    pair = jnp.stack([peak, total])
    for axis, size, dist in rounds:
        other = lax.ppermute(pair, axis, [(j, j ^ dist) for j in range(size)])
        top = jnp.maximum(pair[0], other[0])
        both = pair[1] * jnp.exp(pair[0] - top) + other[1] * jnp.exp(other[0] - top)
        pair = jnp.stack([top, both])
    return pair[0], pair[1]


def ring(axis, size, step):
    return [(j, (j + step) % size) for j in range(size)]


def pick(stack, index):
    return lax.dynamic_index_in_dim(stack, index, axis=0, keepdims=False)


def reduce_rows(summed, row_total, offset, sizes):
    x_size = sizes["x"]
    c, p, z = lax.axis_index("core"), lax.axis_index("x"), lax.axis_index("zl")
    rows, width = summed.shape
    half = rows // 2
    piece = half // (2 * x_size)
    halves = summed.reshape(2, half, width)
    swap = [(0, 1), (1, 0)]
    held = pick(halves, c) + lax.ppermute(pick(halves, 1 - c), "core", swap)
    own = held.reshape(x_size, 2, piece, width)
    right, left = pick(own[:, 0], (p - 1) % x_size), pick(own[:, 1], (p + 1) % x_size)
    for s in range(x_size - 1):
        right = lax.ppermute(right, "x", ring("x", x_size, 1)) + pick(own[:, 0], (p - s - 2) % x_size)
        left = lax.ppermute(left, "x", ring("x", x_size, -1)) + pick(own[:, 1], (p + s + 2) % x_size)
    block = jnp.stack([right, left])
    mine = pick(block, z) + lax.ppermute(pick(block, 1 - z), "zl", swap)
    start = offset + c * half + p * (2 * piece) + z * piece
    mine = mine / lax.dynamic_slice_in_dim(row_total, start, piece)[:, None]
    other = lax.ppermute(mine, "zl", swap)
    block = jnp.where(z == 0, jnp.stack([mine, other]), jnp.stack([other, mine]))
    gathered = jnp.zeros((x_size, 2, piece, width), summed.dtype).at[p].set(block)
    right, left = block[0], block[1]
    for s in range(x_size - 1):
        right = lax.ppermute(right, "x", ring("x", x_size, 1))
        left = lax.ppermute(left, "x", ring("x", x_size, -1))
        gathered = gathered.at[(p - s - 1) % x_size, 0].set(right)
        gathered = gathered.at[(p + s + 1) % x_size, 1].set(left)
    held = gathered.reshape(half, width)
    other = lax.ppermute(held, "core", swap)
    return jnp.where(c == 0, jnp.stack([held, other]), jnp.stack([other, held])).reshape(rows, width)


def gather_features(captions, sizes):
    y_size = sizes["y"]
    rows, width = captions.shape
    h, y = lax.axis_index("zh"), lax.axis_index("y")
    other = lax.ppermute(captions, "zh", [(0, 1), (1, 0)])
    pair = jnp.where(h == 0, jnp.stack([captions, other]), jnp.stack([other, captions]))
    got = jnp.zeros((y_size, 2, rows, width), captions.dtype).at[y].set(pair)
    right, left = pair[0], pair[1]
    for s in range(y_size - 1):
        right = lax.ppermute(right, "y", ring("y", y_size, 1))
        left = lax.ppermute(left, "y", ring("y", y_size, -1))
        got = got.at[(y - s - 1) % y_size, 0].set(right)
        got = got.at[(y + s + 1) % y_size, 1].set(left)
    return got.transpose(1, 0, 3, 2).reshape(2 * y_size * width, rows)


def local(images, captions, bank, sizes):
    img_rounds = [("zh", sizes["zh"], 1)] + [("y", sizes["y"], d) for d in (1, 2)]
    cap_rounds = [("core", sizes["core"], 1), ("zl", sizes["zl"], 1)] + [
        ("x", sizes["x"], d) for d in (1, 2)
    ]
    features = gather_features(captions, sizes)
    querybank_similarity = similar(bank, features)
    local_peak = jnp.max(querybank_similarity, axis=0)
    local_total = jnp.sum(jnp.exp(querybank_similarity - local_peak[None, :]), axis=0)
    raw = lax.optimization_barrier(similar(images, features))
    peak, total = merge_peaks(img_rounds, local_peak, local_total)
    col_log = peak + jnp.log(total)
    logits = raw - col_log[None, :]
    row_peak = jnp.max(logits, axis=1)
    weights = jnp.exp(logits - row_peak[:, None])
    row_sum = jnp.sum(weights, axis=1)
    top, row_total = merge_peaks(cap_rounds, row_peak, row_sum)
    scale = jnp.exp(row_peak - top)
    rows = weights.shape[0]
    chunk = rows // 2
    parts = []
    for k in range(2):
        part = slice(k * chunk, (k + 1) * chunk)
        summed = lax.optimization_barrier(rescaled_affinity(weights[part], features))
        summed = summed * scale[part, None]
        parts.append(reduce_rows(summed, row_total, k * chunk, sizes))
    return jnp.concatenate(parts, axis=0)


def solution(mesh):
    zh, y = 2, mesh.shape["img"] // 2
    zl, core = 2, 2
    x = mesh.shape["cap"] // (zl * core)
    sizes = dict(zh=zh, y=y, x=x, zl=zl, core=core)
    fine = Mesh(mesh.devices.reshape(zh, y, x, zl, core), ("zh", "y", "x", "zl", "core"))

    def run(images, captions, bank):
        return local(images, captions, bank, sizes)

    return jax.shard_map(
        run,
        mesh=fine,
        in_specs=(P(IMG, None), P(CAP, IMG), P(IMG, None)),
        out_specs=P(IMG, None),
        check_vma=False,
    )
```

```python
import jax
import jax.numpy as jnp
from jax import lax
from jax.experimental.layout import Layout, with_layout_constraint
from jax.sharding import Mesh
from jax.sharding import PartitionSpec as P

exponent_divisor = 0.03

IMG = ("zh", "y")
CAP = ("x", "zl", "core")


def similar(query_factor, target_factor):
    product = lax.dot_general(
        query_factor,
        target_factor,
        (((1,), (0,)), ((), ())),
        precision=lax.Precision.HIGHEST,
        preferred_element_type=jnp.float32,
    )
    return exponent_divisor * with_layout_constraint(product, Layout((0, 1)))


def rescaled_affinity(weights, features):
    return lax.dot_general(
        weights,
        features,
        (((1,), (1,)), ((), ())),
        precision=lax.Precision.HIGHEST,
        preferred_element_type=jnp.float32,
    )


def merge_peaks(rounds, peak, total):
    pair = jnp.stack([peak, total])
    for axis, size, dist in rounds:
        other = lax.ppermute(pair, axis, [(j, j ^ dist) for j in range(size)])
        top = jnp.maximum(pair[0], other[0])
        both = pair[1] * jnp.exp(pair[0] - top) + other[1] * jnp.exp(other[0] - top)
        pair = jnp.stack([top, both])
    return pair[0], pair[1]


def ring(axis, size, step):
    return [(j, (j + step) % size) for j in range(size)]


def pick(stack, index):
    return lax.dynamic_index_in_dim(stack, index, axis=0, keepdims=False)


def reduce_rows(summed, row_total, offset, sizes):
    x_size = sizes["x"]
    c, p, z = lax.axis_index("core"), lax.axis_index("x"), lax.axis_index("zl")
    rows, width = summed.shape
    half = rows // 2
    piece = half // (2 * x_size)
    halves = summed.reshape(2, half, width)
    swap = [(0, 1), (1, 0)]
    held = pick(halves, c) + lax.ppermute(pick(halves, 1 - c), "core", swap)
    own = held.reshape(x_size, 2, piece, width)
    right, left = pick(own[:, 0], (p - 1) % x_size), pick(own[:, 1], (p + 1) % x_size)
    for s in range(x_size - 1):
        right = lax.ppermute(right, "x", ring("x", x_size, 1)) + pick(own[:, 0], (p - s - 2) % x_size)
        left = lax.ppermute(left, "x", ring("x", x_size, -1)) + pick(own[:, 1], (p + s + 2) % x_size)
    block = jnp.stack([right, left])
    mine = pick(block, z) + lax.ppermute(pick(block, 1 - z), "zl", swap)
    start = offset + c * half + p * (2 * piece) + z * piece
    mine = mine / lax.dynamic_slice_in_dim(row_total, start, piece)[:, None]
    other = lax.ppermute(mine, "zl", swap)
    block = jnp.where(z == 0, jnp.stack([mine, other]), jnp.stack([other, mine]))
    gathered = jnp.zeros((x_size, 2, piece, width), summed.dtype).at[p].set(block)
    right, left = block[0], block[1]
    for s in range(x_size - 1):
        right = lax.ppermute(right, "x", ring("x", x_size, 1))
        left = lax.ppermute(left, "x", ring("x", x_size, -1))
        gathered = gathered.at[(p - s - 1) % x_size, 0].set(right)
        gathered = gathered.at[(p + s + 1) % x_size, 1].set(left)
    held = gathered.reshape(half, width)
    other = lax.ppermute(held, "core", swap)
    return jnp.where(c == 0, jnp.stack([held, other]), jnp.stack([other, held])).reshape(rows, width)


def gather_features(captions, sizes):
    y_size = sizes["y"]
    rows, width = captions.shape
    h, y = lax.axis_index("zh"), lax.axis_index("y")
    other = lax.ppermute(captions, "zh", [(0, 1), (1, 0)])
    pair = jnp.where(h == 0, jnp.stack([captions, other]), jnp.stack([other, captions]))
    got = jnp.zeros((y_size, 2, rows, width), captions.dtype).at[y].set(pair)
    right, left = pair[0], pair[1]
    for s in range(y_size - 1):
        right = lax.ppermute(right, "y", ring("y", y_size, 1))
        left = lax.ppermute(left, "y", ring("y", y_size, -1))
        got = got.at[(y - s - 1) % y_size, 0].set(right)
        got = got.at[(y + s + 1) % y_size, 1].set(left)
    return got.transpose(1, 0, 3, 2).reshape(2 * y_size * width, rows)


def local(images, captions, bank, sizes):
    img_rounds = [("zh", sizes["zh"], 1)] + [("y", sizes["y"], d) for d in (1, 2)]
    cap_rounds = [("core", sizes["core"], 1), ("zl", sizes["zl"], 1)] + [
        ("x", sizes["x"], d) for d in (1, 2)
    ]
    features = gather_features(captions, sizes)
    querybank_similarity = similar(bank, features)
    local_peak = jnp.max(querybank_similarity, axis=0)
    local_total = jnp.sum(jnp.exp(querybank_similarity - local_peak[None, :]), axis=0)
    split = images.shape[0] // 2
    raw = jnp.concatenate(
        [lax.optimization_barrier(similar(images[:split], features)),
         lax.optimization_barrier(similar(images[split:], features))],
        axis=0,
    )
    peak, total = merge_peaks(img_rounds, local_peak, local_total)
    col_log = peak + jnp.log(total)
    logits = raw - col_log[None, :]
    row_peak = jnp.max(logits, axis=1)
    weights = jnp.exp(logits - row_peak[:, None])
    row_sum = jnp.sum(weights, axis=1)
    top, row_total = merge_peaks(cap_rounds, row_peak, row_sum)
    scale = jnp.exp(row_peak - top)
    rows = weights.shape[0]
    chunk = rows // 2
    parts = []
    for k in range(2):
        part = slice(k * chunk, (k + 1) * chunk)
        summed = lax.optimization_barrier(rescaled_affinity(weights[part], features))
        summed = summed * scale[part, None]
        parts.append(reduce_rows(summed, row_total, k * chunk, sizes))
    return jnp.concatenate(parts, axis=0)


def solution(mesh):
    zh, y = 2, mesh.shape["img"] // 2
    zl, core = 2, 2
    x = mesh.shape["cap"] // (zl * core)
    sizes = dict(zh=zh, y=y, x=x, zl=zl, core=core)
    fine = Mesh(mesh.devices.reshape(zh, y, x, zl, core), ("zh", "y", "x", "zl", "core"))

    def run(images, captions, bank):
        return local(images, captions, bank, sizes)

    return jax.shard_map(
        run,
        mesh=fine,
        in_specs=(P(IMG, None), P(CAP, IMG), P(IMG, None)),
        out_specs=P(IMG, None),
        check_vma=False,
    )
```

```python
import jax
import jax.numpy as jnp
from jax import lax
from jax.experimental.layout import Layout, with_layout_constraint
from jax.sharding import Mesh
from jax.sharding import PartitionSpec as P

exponent_divisor = 0.03

IMG = ("zh", "y")
CAP = ("x", "zl", "core")


def similar(query_factor, target_factor):
    product = lax.dot_general(
        query_factor,
        target_factor,
        (((1,), (0,)), ((), ())),
        precision=lax.Precision.HIGHEST,
        preferred_element_type=jnp.float32,
    )
    return exponent_divisor * with_layout_constraint(product, Layout((0, 1)))


def rescaled_affinity(weights, features):
    return lax.dot_general(
        weights,
        features,
        (((1,), (1,)), ((), ())),
        precision=lax.Precision.HIGHEST,
        preferred_element_type=jnp.float32,
    )


def merge_peaks(rounds, peak, total):
    pair = jnp.stack([peak, total])
    for axis, size, dist in rounds:
        other = lax.ppermute(pair, axis, [(j, j ^ dist) for j in range(size)])
        top = jnp.maximum(pair[0], other[0])
        both = pair[1] * jnp.exp(pair[0] - top) + other[1] * jnp.exp(other[0] - top)
        pair = jnp.stack([top, both])
    return pair[0], pair[1]


def ring(axis, size, step):
    return [(j, (j + step) % size) for j in range(size)]


def pick(stack, index):
    return lax.dynamic_index_in_dim(stack, index, axis=0, keepdims=False)


def reduce_rows(summed, row_total, offset, sizes):
    x_size = sizes["x"]
    c, p, z = lax.axis_index("core"), lax.axis_index("x"), lax.axis_index("zl")
    rows, width = summed.shape
    half = rows // 2
    piece = half // (2 * x_size)
    halves = summed.reshape(2, half, width)
    swap = [(0, 1), (1, 0)]
    held = pick(halves, c) + lax.ppermute(pick(halves, 1 - c), "core", swap)
    own = held.reshape(x_size, 2, piece, width)
    right, left = pick(own[:, 0], (p - 1) % x_size), pick(own[:, 1], (p + 1) % x_size)
    for s in range(x_size - 1):
        right = lax.ppermute(right, "x", ring("x", x_size, 1)) + pick(own[:, 0], (p - s - 2) % x_size)
        left = lax.ppermute(left, "x", ring("x", x_size, -1)) + pick(own[:, 1], (p + s + 2) % x_size)
    block = jnp.stack([right, left])
    mine = pick(block, z) + lax.ppermute(pick(block, 1 - z), "zl", swap)
    start = offset + c * half + p * (2 * piece) + z * piece
    mine = mine / lax.dynamic_slice_in_dim(row_total, start, piece)[:, None]
    other = lax.ppermute(mine, "zl", swap)
    block = jnp.where(z == 0, jnp.stack([mine, other]), jnp.stack([other, mine]))
    gathered = jnp.zeros((x_size, 2, piece, width), summed.dtype).at[p].set(block)
    right, left = block[0], block[1]
    for s in range(x_size - 1):
        right = lax.ppermute(right, "x", ring("x", x_size, 1))
        left = lax.ppermute(left, "x", ring("x", x_size, -1))
        gathered = gathered.at[(p - s - 1) % x_size, 0].set(right)
        gathered = gathered.at[(p + s + 1) % x_size, 1].set(left)
    held = gathered.reshape(half, width)
    other = lax.ppermute(held, "core", swap)
    return jnp.where(c == 0, jnp.stack([held, other]), jnp.stack([other, held])).reshape(rows, width)


def gather_features(captions, sizes):
    y_size = sizes["y"]
    rows, width = captions.shape
    h, y = lax.axis_index("zh"), lax.axis_index("y")
    other = lax.ppermute(captions, "zh", [(0, 1), (1, 0)])
    pair = jnp.where(h == 0, jnp.stack([captions, other]), jnp.stack([other, captions]))
    got = jnp.zeros((y_size, 2, rows, width), captions.dtype).at[y].set(pair)
    right, left = pair[0], pair[1]
    for s in range(y_size - 1):
        right = lax.ppermute(right, "y", ring("y", y_size, 1))
        left = lax.ppermute(left, "y", ring("y", y_size, -1))
        got = got.at[(y - s - 1) % y_size, 0].set(right)
        got = got.at[(y + s + 1) % y_size, 1].set(left)
    return got.transpose(1, 0, 3, 2).reshape(2 * y_size * width, rows)


def local(images, captions, bank, sizes):
    img_rounds = [("zh", sizes["zh"], 1)] + [("y", sizes["y"], d) for d in (1, 2)]
    cap_rounds = [("core", sizes["core"], 1), ("zl", sizes["zl"], 1)] + [
        ("x", sizes["x"], d) for d in (1, 2)
    ]
    features = gather_features(captions, sizes)
    querybank_similarity = similar(bank, features)
    local_peak = jnp.max(querybank_similarity, axis=0)
    local_total = jnp.sum(jnp.exp(querybank_similarity - local_peak[None, :]), axis=0)
    raw = lax.optimization_barrier(similar(images, features))
    peak, total = merge_peaks(img_rounds, local_peak, local_total)
    col_log = peak + jnp.log(total)
    logits = raw - col_log[None, :]
    row_peak = jnp.max(logits, axis=1)
    weights = jnp.exp(logits - row_peak[:, None])
    row_sum = jnp.sum(weights, axis=1)
    top, row_total = merge_peaks(cap_rounds, row_peak, row_sum)
    scale = jnp.exp(row_peak - top)
    rows = weights.shape[0]
    chunk = rows // 2
    parts = []
    for k in range(2):
        part = slice(k * chunk, (k + 1) * chunk)
        quarter = chunk // 2
        summed = jnp.concatenate(
            [lax.optimization_barrier(rescaled_affinity(weights[k * chunk + j * quarter:][:quarter], features))
             for j in range(2)],
            axis=0,
        )
        summed = summed * scale[part, None]
        parts.append(reduce_rows(summed, row_total, k * chunk, sizes))
    return jnp.concatenate(parts, axis=0)


def solution(mesh):
    zh, y = 2, mesh.shape["img"] // 2
    zl, core = 2, 2
    x = mesh.shape["cap"] // (zl * core)
    sizes = dict(zh=zh, y=y, x=x, zl=zl, core=core)
    fine = Mesh(mesh.devices.reshape(zh, y, x, zl, core), ("zh", "y", "x", "zl", "core"))

    def run(images, captions, bank):
        return local(images, captions, bank, sizes)

    return jax.shard_map(
        run,
        mesh=fine,
        in_specs=(P(IMG, None), P(CAP, IMG), P(IMG, None)),
        out_specs=P(IMG, None),
        check_vma=False,
    )
```

```python
import jax
import jax.numpy as jnp
from jax import lax
from jax.experimental.layout import Layout, with_layout_constraint
from jax.sharding import Mesh
from jax.sharding import PartitionSpec as P

exponent_divisor = 0.03

IMG = ("zh", "y")
CAP = ("x", "zl", "core")


def similar(query_factor, target_factor):
    product = lax.dot_general(
        query_factor,
        target_factor,
        (((1,), (0,)), ((), ())),
        precision=lax.Precision.HIGHEST,
        preferred_element_type=jnp.float32,
    )
    return exponent_divisor * with_layout_constraint(product, Layout((0, 1)))


def rescaled_affinity(weights, features):
    return lax.dot_general(
        weights,
        features,
        (((1,), (1,)), ((), ())),
        precision=lax.Precision.HIGHEST,
        preferred_element_type=jnp.float32,
    )


def merge_peaks(rounds, peak, total):
    pair = jnp.stack([peak, total])
    for axis, size, dist in rounds:
        other = lax.ppermute(pair, axis, [(j, j ^ dist) for j in range(size)])
        top = jnp.maximum(pair[0], other[0])
        both = pair[1] * jnp.exp(pair[0] - top) + other[1] * jnp.exp(other[0] - top)
        pair = jnp.stack([top, both])
    return pair[0], pair[1]


def ring(axis, size, step):
    return [(j, (j + step) % size) for j in range(size)]


def pick(stack, index):
    return lax.dynamic_index_in_dim(stack, index, axis=0, keepdims=False)


def reduce_rows(summed, row_total, offset, sizes):
    x_size = sizes["x"]
    c, p, z = lax.axis_index("core"), lax.axis_index("x"), lax.axis_index("zl")
    rows, width = summed.shape
    half = rows // 2
    piece = half // (2 * x_size)
    halves = summed.reshape(2, half, width)
    swap = [(0, 1), (1, 0)]
    held = pick(halves, c) + lax.ppermute(pick(halves, 1 - c), "core", swap)
    own = held.reshape(x_size, 2, piece, width)
    right, left = pick(own[:, 0], (p - 1) % x_size), pick(own[:, 1], (p + 1) % x_size)
    for s in range(x_size - 1):
        right = lax.ppermute(right, "x", ring("x", x_size, 1)) + pick(own[:, 0], (p - s - 2) % x_size)
        left = lax.ppermute(left, "x", ring("x", x_size, -1)) + pick(own[:, 1], (p + s + 2) % x_size)
    block = jnp.stack([right, left])
    mine = pick(block, z) + lax.ppermute(pick(block, 1 - z), "zl", swap)
    start = offset + c * half + p * (2 * piece) + z * piece
    mine = mine / lax.dynamic_slice_in_dim(row_total, start, piece)[:, None]
    other = lax.ppermute(mine, "zl", swap)
    block = jnp.where(z == 0, jnp.stack([mine, other]), jnp.stack([other, mine]))
    gathered = jnp.zeros((x_size, 2, piece, width), summed.dtype).at[p].set(block)
    right, left = block[0], block[1]
    for s in range(x_size - 1):
        right = lax.ppermute(right, "x", ring("x", x_size, 1))
        left = lax.ppermute(left, "x", ring("x", x_size, -1))
        gathered = gathered.at[(p - s - 1) % x_size, 0].set(right)
        gathered = gathered.at[(p + s + 1) % x_size, 1].set(left)
    return gathered.reshape(half, width)


def gather_features(captions, sizes):
    y_size = sizes["y"]
    rows, width = captions.shape
    h, y = lax.axis_index("zh"), lax.axis_index("y")
    other = lax.ppermute(captions, "zh", [(0, 1), (1, 0)])
    pair = jnp.where(h == 0, jnp.stack([captions, other]), jnp.stack([other, captions]))
    got = jnp.zeros((y_size, 2, rows, width), captions.dtype).at[y].set(pair)
    right, left = pair[0], pair[1]
    for s in range(y_size - 1):
        right = lax.ppermute(right, "y", ring("y", y_size, 1))
        left = lax.ppermute(left, "y", ring("y", y_size, -1))
        got = got.at[(y - s - 1) % y_size, 0].set(right)
        got = got.at[(y + s + 1) % y_size, 1].set(left)
    return got.transpose(1, 0, 3, 2).reshape(2 * y_size * width, rows)


def local(images, captions, bank, sizes):
    img_rounds = [("zh", sizes["zh"], 1)] + [("y", sizes["y"], d) for d in (1, 2)]
    cap_rounds = [("core", sizes["core"], 1), ("zl", sizes["zl"], 1)] + [
        ("x", sizes["x"], d) for d in (1, 2)
    ]
    features = gather_features(captions, sizes)
    querybank_similarity = similar(bank, features)
    local_peak = jnp.max(querybank_similarity, axis=0)
    local_total = jnp.sum(jnp.exp(querybank_similarity - local_peak[None, :]), axis=0)
    raw = lax.optimization_barrier(similar(images, features))
    peak, total = merge_peaks(img_rounds, local_peak, local_total)
    col_log = peak + jnp.log(total)
    logits = raw - col_log[None, :]
    row_peak = jnp.max(logits, axis=1)
    weights = jnp.exp(logits - row_peak[:, None])
    row_sum = jnp.sum(weights, axis=1)
    top, row_total = merge_peaks(cap_rounds, row_peak, row_sum)
    scale = jnp.exp(row_peak - top)
    rows = weights.shape[0]
    chunk = rows // 2
    parts = []
    for k in range(2):
        part = slice(k * chunk, (k + 1) * chunk)
        summed = lax.optimization_barrier(rescaled_affinity(weights[part], features))
        summed = summed * scale[part, None]
        parts.append(reduce_rows(summed, row_total, k * chunk, sizes))
    held = jnp.stack(parts)
    other = jnp.stack([lax.ppermute(part, "core", [(0, 1), (1, 0)]) for part in parts])
    c = lax.axis_index("core")
    both = jnp.where(c == 0, jnp.stack([held, other], axis=1), jnp.stack([other, held], axis=1))
    return both.reshape(rows, held.shape[-1])


def solution(mesh):
    zh, y = 2, mesh.shape["img"] // 2
    zl, core = 2, 2
    x = mesh.shape["cap"] // (zl * core)
    sizes = dict(zh=zh, y=y, x=x, zl=zl, core=core)
    fine = Mesh(mesh.devices.reshape(zh, y, x, zl, core), ("zh", "y", "x", "zl", "core"))

    def run(images, captions, bank):
        return local(images, captions, bank, sizes)

    return jax.shard_map(
        run,
        mesh=fine,
        in_specs=(P(IMG, None), P(CAP, IMG), P(IMG, None)),
        out_specs=P(IMG, None),
        check_vma=False,
    )
```

```python
import jax
import jax.numpy as jnp
from jax import lax
from jax.experimental.layout import Layout, with_layout_constraint
from jax.sharding import Mesh
from jax.sharding import PartitionSpec as P

exponent_divisor = 0.03

IMG = ("zh", "y")
CAP = ("x", "zl", "core")


def similar(query_factor, target_factor):
    product = lax.dot_general(
        query_factor,
        target_factor,
        (((1,), (0,)), ((), ())),
        precision=lax.Precision.HIGHEST,
        preferred_element_type=jnp.float32,
    )
    return exponent_divisor * with_layout_constraint(product, Layout((0, 1)))


def rescaled_affinity(weights, features):
    return lax.dot_general(
        weights,
        features,
        (((1,), (1,)), ((), ())),
        precision=lax.Precision.HIGHEST,
        preferred_element_type=jnp.float32,
    )


def merge_peaks(rounds, peak, total):
    pair = jnp.stack([peak, total])
    for axis, size, dist in rounds:
        other = lax.ppermute(pair, axis, [(j, j ^ dist) for j in range(size)])
        top = jnp.maximum(pair[0], other[0])
        both = pair[1] * jnp.exp(pair[0] - top) + other[1] * jnp.exp(other[0] - top)
        pair = jnp.stack([top, both])
    return pair[0], pair[1]


def ring(axis, size, step):
    return [(j, (j + step) % size) for j in range(size)]


def pick(stack, index):
    return lax.dynamic_index_in_dim(stack, index, axis=0, keepdims=False)


def reduce_rows(summed, row_total, offset, sizes):
    x_size = sizes["x"]
    c, p, z = lax.axis_index("core"), lax.axis_index("x"), lax.axis_index("zl")
    rows, width = summed.shape
    half = rows // 2
    piece = half // (2 * x_size)
    halves = summed.reshape(2, half, width)
    swap = [(0, 1), (1, 0)]
    held = pick(halves, c) + lax.ppermute(pick(halves, 1 - c), "core", swap)
    own = held.reshape(x_size, 2, piece, width)
    right, left = pick(own[:, 0], (p - 1) % x_size), pick(own[:, 1], (p + 1) % x_size)
    for s in range(x_size - 1):
        right = lax.ppermute(right, "x", ring("x", x_size, 1)) + pick(own[:, 0], (p - s - 2) % x_size)
        left = lax.ppermute(left, "x", ring("x", x_size, -1)) + pick(own[:, 1], (p + s + 2) % x_size)
    block = jnp.stack([right, left])
    mine = pick(block, z) + lax.ppermute(pick(block, 1 - z), "zl", swap)
    start = offset + c * half + p * (2 * piece) + z * piece
    mine = mine / lax.dynamic_slice_in_dim(row_total, start, piece)[:, None]
    other = lax.ppermute(mine, "zl", swap)
    block = jnp.where(z == 0, jnp.stack([mine, other]), jnp.stack([other, mine]))
    gathered = jnp.zeros((x_size, 2, piece, width), summed.dtype).at[p].set(block)
    right, left = block[0], block[1]
    for s in range(x_size - 1):
        right = lax.ppermute(right, "x", ring("x", x_size, 1))
        left = lax.ppermute(left, "x", ring("x", x_size, -1))
        gathered = gathered.at[(p - s - 1) % x_size, 0].set(right)
        gathered = gathered.at[(p + s + 1) % x_size, 1].set(left)
    held = gathered.reshape(half, width)
    other = lax.ppermute(held, "core", swap)
    return jnp.where(c == 0, jnp.stack([held, other]), jnp.stack([other, held])).reshape(rows, width)


def gather_features(captions, sizes):
    y_size = sizes["y"]
    rows, width = captions.shape
    h, y = lax.axis_index("zh"), lax.axis_index("y")
    other = lax.ppermute(captions, "zh", [(0, 1), (1, 0)])
    pair = jnp.where(h == 0, jnp.stack([captions, other]), jnp.stack([other, captions]))
    got = jnp.zeros((y_size, 2, rows, width), captions.dtype).at[y].set(pair)
    right, left = pair[0], pair[1]
    for s in range(y_size - 1):
        right = lax.ppermute(right, "y", ring("y", y_size, 1))
        left = lax.ppermute(left, "y", ring("y", y_size, -1))
        got = got.at[(y - s - 1) % y_size, 0].set(right)
        got = got.at[(y + s + 1) % y_size, 1].set(left)
    return got.transpose(1, 0, 3, 2).reshape(2 * y_size * width, rows)


def local(images, captions, bank, sizes):
    img_rounds = [("zh", sizes["zh"], 1)] + [("y", sizes["y"], d) for d in (1, 2)]
    cap_rounds = [("core", sizes["core"], 1), ("zl", sizes["zl"], 1)] + [
        ("x", sizes["x"], d) for d in (1, 2)
    ]
    features = gather_features(captions, sizes)
    querybank_similarity = similar(bank, features)
    local_peak = jnp.max(querybank_similarity, axis=0)
    local_total = jnp.sum(jnp.exp(querybank_similarity - local_peak[None, :]), axis=0)
    raw = lax.optimization_barrier(similar(images, features))
    peak, total = merge_peaks(img_rounds, local_peak, local_total)
    col_log = peak + jnp.log(total)
    logits = raw - col_log[None, :]
    row_peak = jnp.max(logits, axis=1)
    weights = jnp.exp(logits - row_peak[:, None])
    row_sum = jnp.sum(weights, axis=1)
    top, row_total = merge_peaks(cap_rounds, row_peak, row_sum)
    scale = jnp.exp(row_peak - top)
    rows = weights.shape[0]
    first = 3 * rows // 8
    bounds = ((0, first), (first, rows))
    parts = []
    for lo, hi in bounds:
        part = slice(lo, hi)
        summed = lax.optimization_barrier(rescaled_affinity(weights[part], features))
        summed = summed * scale[part, None]
        parts.append(reduce_rows(summed, row_total, lo, sizes))
    return jnp.concatenate(parts, axis=0)


def solution(mesh):
    zh, y = 2, mesh.shape["img"] // 2
    zl, core = 2, 2
    x = mesh.shape["cap"] // (zl * core)
    sizes = dict(zh=zh, y=y, x=x, zl=zl, core=core)
    fine = Mesh(mesh.devices.reshape(zh, y, x, zl, core), ("zh", "y", "x", "zl", "core"))

    def run(images, captions, bank):
        return local(images, captions, bank, sizes)

    return jax.shard_map(
        run,
        mesh=fine,
        in_specs=(P(IMG, None), P(CAP, IMG), P(IMG, None)),
        out_specs=P(IMG, None),
        check_vma=False,
    )
```

```python
import jax
import jax.numpy as jnp
from jax import lax
from jax.experimental.layout import Layout, with_layout_constraint
from jax.sharding import Mesh
from jax.sharding import PartitionSpec as P

exponent_divisor = 0.03

IMG = ("zh", "y")
CAP = ("x", "zl", "core")


def similar(query_factor, target_factor):
    product = lax.dot_general(
        query_factor,
        target_factor,
        (((1,), (0,)), ((), ())),
        precision=lax.Precision.HIGHEST,
        preferred_element_type=jnp.float32,
    )
    return exponent_divisor * with_layout_constraint(product, Layout((0, 1)))


def rescaled_affinity(weights, features):
    return lax.dot_general(
        weights,
        features,
        (((1,), (1,)), ((), ())),
        precision=lax.Precision.HIGHEST,
        preferred_element_type=jnp.float32,
    )


def merge_peaks(rounds, peak, total):
    pair = jnp.stack([peak, total])
    for axis, size, dist in rounds:
        other = lax.ppermute(pair, axis, [(j, j ^ dist) for j in range(size)])
        top = jnp.maximum(pair[0], other[0])
        both = pair[1] * jnp.exp(pair[0] - top) + other[1] * jnp.exp(other[0] - top)
        pair = jnp.stack([top, both])
    return pair[0], pair[1]


def ring(axis, size, step):
    return [(j, (j + step) % size) for j in range(size)]


def pick(stack, index):
    return lax.dynamic_index_in_dim(stack, index, axis=0, keepdims=False)


def reduce_rows(summed, row_total, offset, sizes):
    x_size = sizes["x"]
    c, p, z = lax.axis_index("core"), lax.axis_index("x"), lax.axis_index("zl")
    rows, width = summed.shape
    half = rows // 2
    piece = half // (2 * x_size)
    halves = summed.reshape(2, half, width)
    swap = [(0, 1), (1, 0)]
    held = pick(halves, c) + lax.ppermute(pick(halves, 1 - c), "core", swap)
    own = held.reshape(x_size, 2, piece, width)
    right, left = pick(own[:, 0], (p - 1) % x_size), pick(own[:, 1], (p + 1) % x_size)
    for s in range(x_size - 1):
        right = lax.ppermute(right, "x", ring("x", x_size, 1)) + pick(own[:, 0], (p - s - 2) % x_size)
        left = lax.ppermute(left, "x", ring("x", x_size, -1)) + pick(own[:, 1], (p + s + 2) % x_size)
    block = jnp.stack([right, left])
    mine = pick(block, z) + lax.ppermute(pick(block, 1 - z), "zl", swap)
    start = offset + c * half + p * (2 * piece) + z * piece
    mine = mine / lax.dynamic_slice_in_dim(row_total, start, piece)[:, None]
    other = lax.ppermute(mine, "zl", swap)
    block = jnp.where(z == 0, jnp.stack([mine, other]), jnp.stack([other, mine]))
    gathered = jnp.zeros((x_size, 2, piece, width), summed.dtype).at[p].set(block)
    right, left = block[0], block[1]
    for s in range(x_size - 1):
        right = lax.ppermute(right, "x", ring("x", x_size, 1))
        left = lax.ppermute(left, "x", ring("x", x_size, -1))
        gathered = gathered.at[(p - s - 1) % x_size, 0].set(right)
        gathered = gathered.at[(p + s + 1) % x_size, 1].set(left)
    return gathered.reshape(half, width)


def gather_features(captions, sizes):
    y_size = sizes["y"]
    rows, width = captions.shape
    h, y = lax.axis_index("zh"), lax.axis_index("y")
    other = lax.ppermute(captions, "zh", [(0, 1), (1, 0)])
    pair = jnp.where(h == 0, jnp.stack([captions, other]), jnp.stack([other, captions]))
    got = jnp.zeros((y_size, 2, rows, width), captions.dtype).at[y].set(pair)
    right, left = captions, other
    for s in range(y_size - 1):
        right = lax.ppermute(right, "y", ring("y", y_size, 1))
        left = lax.ppermute(left, "y", ring("y", y_size, -1))
        got = lax.dynamic_update_slice(got, right[None, None], ((y - s - 1) % y_size, h, 0, 0))
        got = lax.dynamic_update_slice(got, left[None, None], ((y + s + 1) % y_size, 1 - h, 0, 0))
    return got.transpose(1, 0, 3, 2).reshape(2 * y_size * width, rows)


def local(images, captions, bank, sizes):
    img_rounds = [("zh", sizes["zh"], 1)] + [("y", sizes["y"], d) for d in (1, 2)]
    cap_rounds = [("core", sizes["core"], 1), ("zl", sizes["zl"], 1)] + [
        ("x", sizes["x"], d) for d in (1, 2)
    ]
    features = gather_features(captions, sizes)
    querybank_similarity = similar(bank, features)
    local_peak = jnp.max(querybank_similarity, axis=0)
    local_total = jnp.sum(jnp.exp(querybank_similarity - local_peak[None, :]), axis=0)
    raw = lax.optimization_barrier(similar(images, features))
    peak, total = merge_peaks(img_rounds, local_peak, local_total)
    col_log = peak + jnp.log(total)
    logits = raw - col_log[None, :]
    row_peak = jnp.max(logits, axis=1)
    weights = jnp.exp(logits - row_peak[:, None])
    row_sum = jnp.sum(weights, axis=1)
    top, row_total = merge_peaks(cap_rounds, row_peak, row_sum)
    scale = jnp.exp(row_peak - top)
    rows = weights.shape[0]
    chunk = rows // 2
    parts = []
    for k in range(2):
        part = slice(k * chunk, (k + 1) * chunk)
        summed = lax.optimization_barrier(rescaled_affinity(weights[part], features))
        summed = summed * scale[part, None]
        parts.append(reduce_rows(summed, row_total, k * chunk, sizes))
    held = jnp.stack(parts)
    other = jnp.stack([lax.ppermute(part, "core", [(0, 1), (1, 0)]) for part in parts])
    c = lax.axis_index("core")
    both = jnp.where(c == 0, jnp.stack([held, other], axis=1), jnp.stack([other, held], axis=1))
    return both.reshape(rows, held.shape[-1])


def solution(mesh):
    zh, y = 2, mesh.shape["img"] // 2
    zl, core = 2, 2
    x = mesh.shape["cap"] // (zl * core)
    sizes = dict(zh=zh, y=y, x=x, zl=zl, core=core)
    fine = Mesh(mesh.devices.reshape(zh, y, x, zl, core), ("zh", "y", "x", "zl", "core"))

    def run(images, captions, bank):
        return local(images, captions, bank, sizes)

    return jax.shard_map(
        run,
        mesh=fine,
        in_specs=(P(IMG, None), P(CAP, IMG), P(IMG, None)),
        out_specs=P(IMG, None),
        check_vma=False,
    )
```

```python
import jax
import jax.numpy as jnp
from jax import lax
from jax.experimental.layout import Layout, with_layout_constraint
from jax.sharding import Mesh
from jax.sharding import PartitionSpec as P

exponent_divisor = 0.03

IMG = ("zh", "y")
CAP = ("x", "zl", "core")


def similar(query_factor, target_factor):
    product = lax.dot_general(
        query_factor,
        target_factor,
        (((1,), (0,)), ((), ())),
        precision=lax.Precision.HIGHEST,
        preferred_element_type=jnp.float32,
    )
    return exponent_divisor * with_layout_constraint(product, Layout((0, 1)))


def rescaled_affinity(weights, features):
    return lax.dot_general(
        weights,
        features,
        (((1,), (1,)), ((), ())),
        precision=lax.Precision.HIGHEST,
        preferred_element_type=jnp.float32,
    )


def merge_peaks(rounds, peak, total):
    pair = jnp.stack([peak, total])
    for axis, size, dist in rounds:
        other = lax.ppermute(pair, axis, [(j, j ^ dist) for j in range(size)])
        top = jnp.maximum(pair[0], other[0])
        both = pair[1] * jnp.exp(pair[0] - top) + other[1] * jnp.exp(other[0] - top)
        pair = jnp.stack([top, both])
    return pair[0], pair[1]


def ring(axis, size, step):
    return [(j, (j + step) % size) for j in range(size)]


def pick(stack, index):
    return lax.dynamic_index_in_dim(stack, index, axis=0, keepdims=False)


def reduce_rows(summed, row_total, offset, sizes):
    x_size = sizes["x"]
    c, p, z = lax.axis_index("core"), lax.axis_index("x"), lax.axis_index("zl")
    rows, width = summed.shape
    half = rows // 2
    piece = half // (2 * x_size)
    halves = summed.reshape(2, half, width)
    swap = [(0, 1), (1, 0)]
    held = pick(halves, c) + lax.ppermute(pick(halves, 1 - c), "core", swap)
    own = held.reshape(x_size, 2, piece, width)
    right, left = pick(own[:, 0], (p - 1) % x_size), pick(own[:, 1], (p + 1) % x_size)
    for s in range(x_size - 1):
        right = lax.ppermute(right, "x", ring("x", x_size, 1)) + pick(own[:, 0], (p - s - 2) % x_size)
        left = lax.ppermute(left, "x", ring("x", x_size, -1)) + pick(own[:, 1], (p + s + 2) % x_size)
    block = jnp.stack([right, left])
    mine = pick(block, z) + lax.ppermute(pick(block, 1 - z), "zl", swap)
    start = offset + c * half + p * (2 * piece) + z * piece
    mine = mine / lax.dynamic_slice_in_dim(row_total, start, piece)[:, None]
    other = lax.ppermute(mine, "zl", swap)
    block = jnp.where(z == 0, jnp.stack([mine, other]), jnp.stack([other, mine]))
    gathered = jnp.zeros((x_size, 2, piece, width), summed.dtype).at[p].set(block)
    right, left = block[0], block[1]
    for s in range(x_size - 1):
        right = lax.ppermute(right, "x", ring("x", x_size, 1))
        left = lax.ppermute(left, "x", ring("x", x_size, -1))
        gathered = gathered.at[(p - s - 1) % x_size, 0].set(right)
        gathered = gathered.at[(p + s + 1) % x_size, 1].set(left)
    return gathered.reshape(half, width)


def gather_features(captions, sizes):
    y_size = sizes["y"]
    rows, width = captions.shape
    h, y = lax.axis_index("zh"), lax.axis_index("y")
    other = lax.ppermute(captions, "zh", [(0, 1), (1, 0)])
    pair = jnp.where(h == 0, jnp.stack([captions, other]), jnp.stack([other, captions]))
    got = jnp.zeros((y_size, 2, rows, width), captions.dtype).at[y].set(pair)
    right, left = captions, other
    for s in range(y_size - 1):
        right = lax.ppermute(right, "y", ring("y", y_size, 1))
        left = lax.ppermute(left, "y", ring("y", y_size, -1))
        got = lax.dynamic_update_slice(got, right[None, None], ((y - s - 1) % y_size, h, 0, 0))
        got = lax.dynamic_update_slice(got, left[None, None], ((y + s + 1) % y_size, 1 - h, 0, 0))
    return got.transpose(1, 0, 3, 2).reshape(2 * y_size * width, rows)


def local(images, captions, bank, sizes):
    img_rounds = [("y", sizes["y"], d) for d in (1, 2)] + [("zh", sizes["zh"], 1)]
    cap_rounds = [("core", sizes["core"], 1), ("zl", sizes["zl"], 1)] + [
        ("x", sizes["x"], d) for d in (1, 2)
    ]
    features = gather_features(captions, sizes)
    querybank_similarity = similar(bank, features)
    local_peak = jnp.max(querybank_similarity, axis=0)
    local_total = jnp.sum(jnp.exp(querybank_similarity - local_peak[None, :]), axis=0)
    raw = lax.optimization_barrier(similar(images, features))
    peak, total = merge_peaks(img_rounds, local_peak, local_total)
    col_log = peak + jnp.log(total)
    logits = raw - col_log[None, :]
    row_peak = jnp.max(logits, axis=1)
    weights = jnp.exp(logits - row_peak[:, None])
    row_sum = jnp.sum(weights, axis=1)
    top, row_total = merge_peaks(cap_rounds, row_peak, row_sum)
    scale = jnp.exp(row_peak - top)
    rows = weights.shape[0]
    chunk = rows // 2
    parts = []
    for k in range(2):
        part = slice(k * chunk, (k + 1) * chunk)
        summed = lax.optimization_barrier(rescaled_affinity(weights[part], features))
        summed = summed * scale[part, None]
        parts.append(reduce_rows(summed, row_total, k * chunk, sizes))
    held = jnp.stack(parts)
    other = jnp.stack([lax.ppermute(part, "core", [(0, 1), (1, 0)]) for part in parts])
    c = lax.axis_index("core")
    both = jnp.where(c == 0, jnp.stack([held, other], axis=1), jnp.stack([other, held], axis=1))
    return both.reshape(rows, held.shape[-1])


def solution(mesh):
    zh, y = 2, mesh.shape["img"] // 2
    zl, core = 2, 2
    x = mesh.shape["cap"] // (zl * core)
    sizes = dict(zh=zh, y=y, x=x, zl=zl, core=core)
    fine = Mesh(mesh.devices.reshape(zh, y, x, zl, core), ("zh", "y", "x", "zl", "core"))

    def run(images, captions, bank):
        return local(images, captions, bank, sizes)

    return jax.shard_map(
        run,
        mesh=fine,
        in_specs=(P(IMG, None), P(CAP, IMG), P(IMG, None)),
        out_specs=P(IMG, None),
        check_vma=False,
    )
```
